1024 devices in a mesh: kloop: 256 (over z, y_hi, x), pair: 4 (over y_lo, core).
Axes of the slice: x: 4, y: 8 (y_hi: 4, y_lo: 2; y = y_hi * 2 + y_lo), z: 16, core: 2. Of those that a mesh axis runs over, the one named last changes fastest.
Arguments:
- orbitals: bfloat16 [512, 32, 512], P('kloop'), may hold values from -6 to 6
- fitting: bfloat16 [512, 1400], replicated, may hold values from -0.25 to 0.25
- screen: bfloat16 [4, 1400, 1400], P(None, None, 'pair'), may hold values from -0.00390625 to 0.00390625
- coulomb: float32 [1400], replicated, may hold values from 0.005 to 0.1
- qindex: int32 [512, 2], replicated, may hold values from 0 to 3
Outputs:
- kernel: bfloat16 [512, 2, 256, 256], P('kloop', None, 'pair')
The draws below stay inside these ranges and needn't reach their ends.
Inputs may be any that keep to these rules, and one draw needn't show every extreme that they name: `qindex`: the index of the held screened interaction for each block.
All inputs are finite; a program needn't handle non-finite values.
Results may differ from the reference program's by a relative error of at most 0.0085.
Values may be sent and summed in bfloat16 or wider, within the bound.
No kernel may reach another device: no remote copies, remote signals or barrier semaphores. Data moves between devices by JAX's collectives and lax.ppermute only.
A program may use at most 64 MiB of HBM per device.

```python
import math
import jax
import jax.numpy as jnp
from jax import lax

NV = 16
NC = 16
NB = 32
NG = 1400
MU = 512
NQ = 4
S = 2
K_DEV = 2
K = 512
N_KLOOP = 256
N_PAIR = 4


def with_ends(drawn, own_key, least, high):
    longest = drawn.shape.index(max(drawn.shape))
    spots = []
    for shift in (0, 1):
        where = [jax.random.randint(jax.random.fold_in(own_key, axis), (), 0, length) for axis, length in enumerate(drawn.shape)]
        where[longest] = (where[longest] + shift) % drawn.shape[longest]
        spots.append(tuple(where))
    return drawn.at[spots[0]].set(least).at[spots[1]].set(high)


def steps_of(key, extent, cuts, smallest, largest):
    gain, own = 1.0, jax.random.fold_in(key, 6)
    for position, blocks in cuts:
        heights = jnp.exp(jax.random.uniform(jax.random.fold_in(own, position), (blocks,), jnp.float32, smallest / len(cuts), largest / len(cuts)))
        gain = gain * jnp.repeat(heights, extent[position] // blocks).reshape([-1 if axis == position else 1 for axis in range(len(extent))])
    return gain


def bell_draw(rng, extent, width, limit, shards=(), held_as=jnp.bfloat16):
    values = jax.random.normal(rng, extent, jnp.float32) * width
    if len(shards) > 0:
        values = steps_of(rng, extent, shards, -0.22, 0.18) * values
    return jnp.clip(values, min=-limit, max=limit).astype(held_as)


def setup_inputs(seed: int = 0) -> dict:
    splits = jax.random.split(jax.random.key(seed), 6)
    orbitals = bell_draw(splits[0], (K, NB, MU), 1.0, 6.0, ((0, 256),))
    fitting = bell_draw(splits[1], (MU, NG), MU ** -0.5, 0.25)
    screen = bell_draw(splits[2], (NQ, NG, NG), (NG * NG) ** -0.5, 0.00390625, ((2, 4),))
    coulomb = jnp.clip(jnp.exp(jax.random.uniform(splits[3], (NG,), jnp.float32, math.log(0.005), math.log(0.1))), 0.005, 0.1)
    qindex = with_ends(jax.random.randint(splits[4], (K, S), 0, NQ), jax.random.fold_in(splits[4], 1), 0, NQ - 1).astype(jnp.int32)
    return {"orbitals": orbitals, "fitting": fitting, "screen": screen, "coulomb": coulomb, "qindex": qindex}


def pair_fields(left_bands, right_bands, fitting):
    products = (left_bands.astype(jnp.float32)[:, None, :] * right_bands.astype(jnp.float32)[None, :, :]).astype(jnp.bfloat16)
    flat = products.reshape(left_bands.shape[0] * right_bands.shape[0], left_bands.shape[1])
    return jnp.dot(flat, fitting, preferred_element_type=jnp.float32).astype(jnp.bfloat16)


def reference(orbitals, fitting, screen, coulomb, qindex):
    kpoints_all = K_DEV * N_KLOOP
    slice_width = NG // N_PAIR

    def own_fields(orbital):
        fields = pair_fields(orbital[:NV], orbital[NV:], fitting)
        weighted = (fields.astype(jnp.float32) * coulomb).astype(jnp.bfloat16)
        return fields, weighted

    own_all, weighted_all = lax.map(own_fields, orbitals)
    results = []
    for shift_step in range(1, S + 1):
        def one_block(column):
            row = (column + shift_step * K_DEV) % kpoints_all
            row_orb = orbitals[row]
            col_orb = orbitals[column]
            cond = pair_fields(row_orb[NV:], col_orb[NV:], fitting)
            vale = pair_fields(row_orb[:NV], col_orb[:NV], fitting)
            interaction = screen[qindex[column, shift_step - 1]]
            screened = jnp.dot(cond, interaction, preferred_element_type=jnp.float32).astype(jnp.bfloat16)
            cond_four = screened.astype(jnp.float32).reshape(NC, NC, N_PAIR, slice_width)
            vale_four = vale.astype(jnp.float32).reshape(NV, NV, N_PAIR, slice_width)
            parts = jnp.einsum("xypg,vwpg->pvxwy", cond_four, vale_four).reshape(N_PAIR, NV * NC, NV * NC)
            parts = lax.optimization_barrier(parts.astype(jnp.bfloat16)).astype(jnp.float32)
            direct = jnp.sum(parts, axis=0)
            exchange = lax.dot_general(weighted_all[row], own_all[column], (((1,), (1,)), ((), ())), preferred_element_type=jnp.float32)
            return (2.0 * exchange - direct).astype(jnp.bfloat16)

        results.append(lax.map(one_block, jnp.arange(kpoints_all, dtype=jnp.int32)))
    return jnp.stack(results, axis=1)
```

```python
import jax
import jax.numpy as jnp
from jax import lax
from jax.sharding import PartitionSpec as P

NV = 16
NC = 16
S = 2


def from_behind(value, axis, steps):
    count = lax.axis_size(axis)
    pairs = [(source, (source + steps) % count) for source in range(count)]
    return lax.ppermute(value, axis, pairs)


def products(left_bands, right_bands):
    prod = left_bands.astype(jnp.float32)[..., :, None, :] * right_bands.astype(jnp.float32)[..., None, :, :]
    lead = prod.shape[:-3]
    return prod.astype(jnp.bfloat16).reshape(*lead, prod.shape[-3] * prod.shape[-2], prod.shape[-1])


def fields(left_bands, right_bands, fit):
    prod = products(left_bands, right_bands)
    return jnp.einsum("...pm,mg->...pg", prod, fit, preferred_element_type=jnp.float32).astype(jnp.bfloat16)


def shards(orbitals, fitting, screen, coulomb, qindex):
    per_dev = orbitals.shape[0]
    npair = lax.axis_size("pair")
    pair_index = lax.axis_index("pair")
    loop_index = lax.axis_index("kloop")
    width = screen.shape[2]
    ng = screen.shape[1]
    vr = NV // npair
    fitting_part = lax.dynamic_slice_in_dim(fitting, pair_index * width, width, 1)

    rows = jnp.stack([from_behind(orbitals, "kloop", -s) for s in range(1, S + 1)], 0)
    cols = jnp.broadcast_to(orbitals[None], rows.shape)

    own = fields(orbitals[:, :NV], orbitals[:, NV:], fitting)

    cond = fields(rows[:, :, NV:], cols[:, :, NV:], fitting)
    vale = fields(rows[:, :, :NV], cols[:, :, :NV], fitting_part)

    screen2d = screen.reshape(screen.shape[0] * ng, width)
    screened = []
    for s in range(S):
        row_s = []
        for lk in range(per_dev):
            q = qindex[loop_index * per_dev + lk, s]
            inter = lax.dynamic_slice_in_dim(screen2d, q * ng, ng, 0)
            row_s.append(jnp.dot(cond[s, lk], inter, preferred_element_type=jnp.float32).astype(jnp.bfloat16))
        screened.append(jnp.stack(row_s, 0))
    screened = jnp.stack(screened, 0)

    terms = jnp.einsum("abpg,abqg->abpq", vale, screened, preferred_element_type=jnp.float32).astype(jnp.bfloat16)
    terms = terms.reshape(S, per_dev, npair, vr * NV, NC * NC)
    terms = jnp.moveaxis(terms, 2, 0)
    got = lax.all_to_all(terms, "pair", 0, 0, tiled=True)
    dsum = jnp.sum(got.astype(jnp.float32), axis=0)
    direct = dsum.reshape(S, per_dev, vr, NV, NC, NC).transpose(0, 1, 2, 4, 3, 5).reshape(S, per_dev, vr * NC, NV * NC)

    row_chosen = lax.dynamic_slice_in_dim(rows, pair_index * vr, vr, 2)
    rowf = fields(row_chosen, rows[:, :, NV:], fitting)
    weighted = (rowf.astype(jnp.float32) * coulomb).astype(jnp.bfloat16)
    exchange = jnp.einsum("abpg,bqg->abpq", weighted, own, preferred_element_type=jnp.float32)
    out = (2.0 * exchange - direct).astype(jnp.bfloat16)
    return jnp.swapaxes(out, 0, 1)


def solution(mesh):
    return jax.shard_map(
        shards,
        mesh=mesh,
        in_specs=(P("kloop", None, None), P(), P(None, None, "pair"), P(), P()),
        out_specs=P("kloop", None, "pair", None),
        check_vma=False,
    )
```

```python
import jax
import jax.numpy as jnp
from jax import lax
from jax.sharding import PartitionSpec as P
from jax.experimental import pallas as pl
from jax.experimental.pallas import tpu as pltpu

NV = 16
NC = 16
S = 2


def from_behind(value, axis, steps):
    count = lax.axis_size(axis)
    pairs = [(source, (source + steps) % count) for source in range(count)]
    return lax.ppermute(value, axis, pairs)


def products(left_bands, right_bands):
    prod = left_bands.astype(jnp.float32)[..., :, None, :] * right_bands.astype(jnp.float32)[..., None, :, :]
    lead = prod.shape[:-3]
    return prod.astype(jnp.bfloat16).reshape(*lead, prod.shape[-3] * prod.shape[-2], prod.shape[-1])


def fields(left_bands, right_bands, fit):
    prod = products(left_bands, right_bands)
    return jnp.einsum("...pm,mg->...pg", prod, fit, preferred_element_type=jnp.float32).astype(jnp.bfloat16)


def nt(left, right):
    return lax.dot_general(left, right, (((1,), (1,)), ((), ())), preferred_element_type=jnp.float32)


def direct_kernel(q_ref, cond_pairs_ref, vale_pairs_ref, fit_ref, fit_part_ref, screen_ref, out_ref):
    q = q_ref[pl.program_id(0)]
    cond = nt(cond_pairs_ref[0], fit_ref[...]).astype(jnp.bfloat16)
    inter = lax.switch(q, [lambda i=i: screen_ref[:, i, :] for i in range(screen_ref.shape[1])])
    screened = nt(cond, inter).astype(jnp.bfloat16)
    vale = nt(vale_pairs_ref[0], fit_part_ref[...]).astype(jnp.bfloat16)
    out_ref[0] = nt(vale, screened).astype(jnp.bfloat16)


def direct_terms(q, cond_pairs, vale_pairs, fit_t, fit_part_t, screen_t):
    blocks, rows, mu = cond_pairs.shape
    vrows = vale_pairs.shape[1]
    full = lambda shape: pl.BlockSpec(shape, lambda b, q: (0,) * len(shape))
    return pl.pallas_call(
        direct_kernel,
        out_shape=jax.ShapeDtypeStruct((blocks, vrows, rows), jnp.bfloat16),
        grid_spec=pltpu.PrefetchScalarGridSpec(
            num_scalar_prefetch=1,
            grid=(blocks,),
            in_specs=[
                pl.BlockSpec((1, rows, mu), lambda b, q: (b, 0, 0)),
                pl.BlockSpec((1, vrows, mu), lambda b, q: (b, 0, 0)),
                full(fit_t.shape),
                full(fit_part_t.shape),
                full(screen_t.shape),
            ],
            out_specs=pl.BlockSpec((1, vrows, rows), lambda b, q: (b, 0, 0)),
        ),
    )(q, cond_pairs, vale_pairs, fit_t, fit_part_t, screen_t)


def shards(orbitals, fitting, screen, coulomb, qindex):
    per_dev = orbitals.shape[0]
    npair = lax.axis_size("pair")
    pair_index = lax.axis_index("pair")
    loop_index = lax.axis_index("kloop")
    width = screen.shape[2]
    ng = screen.shape[1]
    vr = NV // npair

    rows = jnp.stack([from_behind(orbitals, "kloop", -s) for s in range(1, S + 1)], 0)
    cols = jnp.broadcast_to(orbitals[None], rows.shape)

    own = fields(orbitals[:, :NV], orbitals[:, NV:], fitting)

    blocks = S * per_dev
    cond_pairs = products(rows[:, :, NV:], cols[:, :, NV:]).reshape(blocks, NC * NC, -1)
    vale_pairs = products(rows[:, :, :NV], cols[:, :, :NV]).reshape(blocks, NV * NV, -1)
    fit_t = fitting.T
    fit_part_t = lax.dynamic_slice_in_dim(fit_t, pair_index * width, width, 0)

    nq = screen.shape[0]
    qs = jnp.stack([qindex[loop_index * per_dev + lk, s] for s in range(S) for lk in range(per_dev)])
    qs = jnp.clip(qs, 0, nq - 1)
    terms = direct_terms(qs, cond_pairs, vale_pairs, fit_t, fit_part_t, jnp.transpose(screen, (2, 0, 1)))
    terms = terms.reshape(S, per_dev, npair, vr * NV, NC * NC)
    terms = jnp.moveaxis(terms, 2, 0)
    got = lax.all_to_all(terms, "pair", 0, 0, tiled=True)
    dsum = jnp.sum(got.astype(jnp.float32), axis=0)
    direct = dsum.reshape(S, per_dev, vr, NV, NC, NC).transpose(0, 1, 2, 4, 3, 5).reshape(S, per_dev, vr * NC, NV * NC)

    row_chosen = lax.dynamic_slice_in_dim(rows, pair_index * vr, vr, 2)
    rowf = fields(row_chosen, rows[:, :, NV:], fitting)
    weighted = (rowf.astype(jnp.float32) * coulomb).astype(jnp.bfloat16)
    exchange = jnp.einsum("abpg,bqg->abpq", weighted, own, preferred_element_type=jnp.float32)
    out = (2.0 * exchange - direct).astype(jnp.bfloat16)
    return jnp.swapaxes(out, 0, 1)


def solution(mesh):
    return jax.shard_map(
        shards,
        mesh=mesh,
        in_specs=(P("kloop", None, None), P(), P(None, None, "pair"), P(), P()),
        out_specs=P("kloop", None, "pair", None),
        check_vma=False,
    )
```

```python
import jax
import jax.numpy as jnp
from jax import lax
from jax.sharding import PartitionSpec as P
from jax.experimental import pallas as pl
from jax.experimental.pallas import tpu as pltpu

NV = 16
NC = 16
S = 2


def from_behind(value, axis, steps):
    count = lax.axis_size(axis)
    pairs = [(source, (source + steps) % count) for source in range(count)]
    return lax.ppermute(value, axis, pairs)


def products(left_bands, right_bands):
    prod = left_bands.astype(jnp.float32)[..., :, None, :] * right_bands.astype(jnp.float32)[..., None, :, :]
    lead = prod.shape[:-3]
    return prod.astype(jnp.bfloat16).reshape(*lead, prod.shape[-3] * prod.shape[-2], prod.shape[-1])


def products_t(left_bands, right_bands):
    left_t = jnp.swapaxes(left_bands, -1, -2).astype(jnp.float32)
    right_t = jnp.swapaxes(right_bands, -1, -2).astype(jnp.float32)
    prod = (left_t[..., :, None] * right_t[..., None, :]).astype(jnp.bfloat16)
    return prod.reshape(*prod.shape[:-2], prod.shape[-2] * prod.shape[-1])


def fields(left_bands, right_bands, fit):
    prod = products(left_bands, right_bands)
    return jnp.einsum("...pm,mg->...pg", prod, fit, preferred_element_type=jnp.float32).astype(jnp.bfloat16)


def nt(left, right):
    return lax.dot_general(left, right, (((1,), (1,)), ((), ())), preferred_element_type=jnp.float32)


def direct_kernel(q_ref, cond_pairs_ref, vale_pairs_ref, fit_ref, fit_part_ref, screen_ref, out_ref):
    q = q_ref[pl.program_id(0)]
    cond_t = jnp.dot(fit_ref[...], cond_pairs_ref[0], preferred_element_type=jnp.float32).astype(jnp.bfloat16)
    inter = lax.switch(q, [lambda i=i: screen_ref[:, i, :] for i in range(screen_ref.shape[1])])
    screened_t = jnp.dot(inter, cond_t, preferred_element_type=jnp.float32).astype(jnp.bfloat16)
    vale_t = jnp.dot(fit_part_ref[...], vale_pairs_ref[0], preferred_element_type=jnp.float32).astype(jnp.bfloat16)
    terms = lax.dot_general(vale_t, screened_t, (((0,), (0,)), ((), ())), preferred_element_type=jnp.float32)
    out_ref[0] = terms.astype(jnp.bfloat16)


def direct_terms(q, cond_pairs, vale_pairs, fit_t, fit_part_t, screen_t):
    blocks, mu, rows = cond_pairs.shape
    vrows = vale_pairs.shape[2]
    full = lambda shape: pl.BlockSpec(shape, lambda b, q: (0,) * len(shape))
    return pl.pallas_call(
        direct_kernel,
        out_shape=jax.ShapeDtypeStruct((blocks, vrows, rows), jnp.bfloat16),
        grid_spec=pltpu.PrefetchScalarGridSpec(
            num_scalar_prefetch=1,
            grid=(blocks,),
            in_specs=[
                pl.BlockSpec((1, mu, rows), lambda b, q: (b, 0, 0)),
                pl.BlockSpec((1, mu, vrows), lambda b, q: (b, 0, 0)),
                full(fit_t.shape),
                full(fit_part_t.shape),
                full(screen_t.shape),
            ],
            out_specs=pl.BlockSpec((1, vrows, rows), lambda b, q: (b, 0, 0)),
        ),
    )(q, cond_pairs, vale_pairs, fit_t, fit_part_t, screen_t)


def shards(orbitals, fitting, screen, coulomb, qindex):
    per_dev = orbitals.shape[0]
    npair = lax.axis_size("pair")
    pair_index = lax.axis_index("pair")
    loop_index = lax.axis_index("kloop")
    width = screen.shape[2]
    ng = screen.shape[1]
    vr = NV // npair

    rows = jnp.stack([from_behind(orbitals, "kloop", -s) for s in range(1, S + 1)], 0)
    cols = jnp.broadcast_to(orbitals[None], rows.shape)

    own = fields(orbitals[:, :NV], orbitals[:, NV:], fitting)

    blocks = S * per_dev
    cond_pairs = products_t(rows[:, :, NV:], cols[:, :, NV:]).reshape(blocks, -1, NC * NC)
    vale_pairs = products_t(rows[:, :, :NV], cols[:, :, :NV]).reshape(blocks, -1, NV * NV)
    fit_t = fitting.T
    fit_part_t = lax.dynamic_slice_in_dim(fit_t, pair_index * width, width, 0)

    nq = screen.shape[0]
    qs = jnp.stack([qindex[loop_index * per_dev + lk, s] for s in range(S) for lk in range(per_dev)])
    qs = jnp.clip(qs, 0, nq - 1)
    terms = direct_terms(qs, cond_pairs, vale_pairs, fit_t, fit_part_t, jnp.transpose(screen, (2, 0, 1)))
    terms = terms.reshape(S, per_dev, npair, vr * NV, NC * NC)
    terms = jnp.moveaxis(terms, 2, 0)
    got = lax.all_to_all(terms, "pair", 0, 0, tiled=True)
    dsum = jnp.sum(got.astype(jnp.float32), axis=0)
    direct = dsum.reshape(S, per_dev, vr, NV, NC, NC).transpose(0, 1, 2, 4, 3, 5).reshape(S, per_dev, vr * NC, NV * NC)

    row_chosen = lax.dynamic_slice_in_dim(rows, pair_index * vr, vr, 2)
    rowf = fields(row_chosen, rows[:, :, NV:], fitting)
    weighted = (rowf.astype(jnp.float32) * coulomb).astype(jnp.bfloat16)
    exchange = jnp.einsum("abpg,bqg->abpq", weighted, own, preferred_element_type=jnp.float32)
    out = (2.0 * exchange - direct).astype(jnp.bfloat16)
    return jnp.swapaxes(out, 0, 1)


def solution(mesh):
    return jax.shard_map(
        shards,
        mesh=mesh,
        in_specs=(P("kloop", None, None), P(), P(None, None, "pair"), P(), P()),
        out_specs=P("kloop", None, "pair", None),
        check_vma=False,
    )
```

```python
import jax
import jax.numpy as jnp
from jax import lax
from jax.sharding import PartitionSpec as P
from jax.experimental import pallas as pl
from jax.experimental.pallas import tpu as pltpu

NV = 16
NC = 16
S = 2


def from_behind(value, axis, steps):
    count = lax.axis_size(axis)
    pairs = [(source, (source + steps) % count) for source in range(count)]
    return lax.ppermute(value, axis, pairs)


def products(left_bands, right_bands):
    prod = left_bands.astype(jnp.float32)[..., :, None, :] * right_bands.astype(jnp.float32)[..., None, :, :]
    lead = prod.shape[:-3]
    return prod.astype(jnp.bfloat16).reshape(*lead, prod.shape[-3] * prod.shape[-2], prod.shape[-1])


def products_t(left_bands, right_bands):
    left_t = jnp.swapaxes(left_bands, -1, -2).astype(jnp.float32)
    right_t = jnp.swapaxes(right_bands, -1, -2).astype(jnp.float32)
    prod = (left_t[..., :, None] * right_t[..., None, :]).astype(jnp.bfloat16)
    return prod.reshape(*prod.shape[:-2], prod.shape[-2] * prod.shape[-1])


def fields(left_bands, right_bands, fit):
    prod = products(left_bands, right_bands)
    return jnp.einsum("...pm,mg->...pg", prod, fit, preferred_element_type=jnp.float32).astype(jnp.bfloat16)


def nt(left, right):
    return lax.dot_general(left, right, (((1,), (1,)), ((), ())), preferred_element_type=jnp.float32)


def direct_kernel(q_ref, cond_pairs_ref, vale_pairs_ref, fit_ref, fit_part_ref, screen_ref, out_ref):
    q = q_ref[pl.program_id(0)]
    cond_t = jnp.dot(fit_ref[...], cond_pairs_ref[0], preferred_element_type=jnp.float32).astype(jnp.bfloat16)
    every = jnp.dot(screen_ref[...], cond_t, preferred_element_type=jnp.float32).astype(jnp.bfloat16)
    width = fit_part_ref.shape[0]
    row = lax.broadcasted_iota(jnp.int32, (width, screen_ref.shape[0]), 0)
    col = lax.broadcasted_iota(jnp.int32, (width, screen_ref.shape[0]), 1)
    pick = jnp.where(col == row * (screen_ref.shape[0] // width) + q, 1.0, 0.0).astype(jnp.bfloat16)
    screened_t = jnp.dot(pick, every, preferred_element_type=jnp.float32).astype(jnp.bfloat16)
    vale_t = jnp.dot(fit_part_ref[...], vale_pairs_ref[0], preferred_element_type=jnp.float32).astype(jnp.bfloat16)
    terms = lax.dot_general(vale_t, screened_t, (((0,), (0,)), ((), ())), preferred_element_type=jnp.float32)
    out_ref[0] = terms.astype(jnp.bfloat16)


def direct_terms(q, cond_pairs, vale_pairs, fit_t, fit_part_t, screen_t):
    blocks, mu, rows = cond_pairs.shape
    vrows = vale_pairs.shape[2]
    full = lambda shape: pl.BlockSpec(shape, lambda b, q: (0,) * len(shape))
    return pl.pallas_call(
        direct_kernel,
        out_shape=jax.ShapeDtypeStruct((blocks, vrows, rows), jnp.bfloat16),
        grid_spec=pltpu.PrefetchScalarGridSpec(
            num_scalar_prefetch=1,
            grid=(blocks,),
            in_specs=[
                pl.BlockSpec((1, mu, rows), lambda b, q: (b, 0, 0)),
                pl.BlockSpec((1, mu, vrows), lambda b, q: (b, 0, 0)),
                full(fit_t.shape),
                full(fit_part_t.shape),
                full(screen_t.shape),
            ],
            out_specs=pl.BlockSpec((1, vrows, rows), lambda b, q: (b, 0, 0)),
        ),
    )(q, cond_pairs, vale_pairs, fit_t, fit_part_t, screen_t)


def shards(orbitals, fitting, screen, coulomb, qindex):
    per_dev = orbitals.shape[0]
    npair = lax.axis_size("pair")
    pair_index = lax.axis_index("pair")
    loop_index = lax.axis_index("kloop")
    width = screen.shape[2]
    ng = screen.shape[1]
    vr = NV // npair

    rows = jnp.stack([from_behind(orbitals, "kloop", -s) for s in range(1, S + 1)], 0)
    cols = jnp.broadcast_to(orbitals[None], rows.shape)

    own = fields(orbitals[:, :NV], orbitals[:, NV:], fitting)

    blocks = S * per_dev
    cond_pairs = products_t(rows[:, :, NV:], cols[:, :, NV:]).reshape(blocks, -1, NC * NC)
    vale_pairs = products_t(rows[:, :, :NV], cols[:, :, :NV]).reshape(blocks, -1, NV * NV)
    fit_t = fitting.T
    fit_part_t = lax.dynamic_slice_in_dim(fit_t, pair_index * width, width, 0)

    nq = screen.shape[0]
    qs = jnp.stack([qindex[loop_index * per_dev + lk, s] for s in range(S) for lk in range(per_dev)])
    qs = jnp.clip(qs, 0, nq - 1)
    terms = direct_terms(qs, cond_pairs, vale_pairs, fit_t, fit_part_t, jnp.transpose(screen, (2, 0, 1)).reshape(width * nq, ng))
    terms = terms.reshape(S, per_dev, npair, vr * NV, NC * NC)
    terms = jnp.moveaxis(terms, 2, 0)
    got = lax.all_to_all(terms, "pair", 0, 0, tiled=True)
    dsum = jnp.sum(got.astype(jnp.float32), axis=0)
    direct = dsum.reshape(S, per_dev, vr, NV, NC, NC).transpose(0, 1, 2, 4, 3, 5).reshape(S, per_dev, vr * NC, NV * NC)

    row_chosen = lax.dynamic_slice_in_dim(rows, pair_index * vr, vr, 2)
    rowf = fields(row_chosen, rows[:, :, NV:], fitting)
    weighted = (rowf.astype(jnp.float32) * coulomb).astype(jnp.bfloat16)
    exchange = jnp.einsum("abpg,bqg->abpq", weighted, own, preferred_element_type=jnp.float32)
    out = (2.0 * exchange - direct).astype(jnp.bfloat16)
    return jnp.swapaxes(out, 0, 1)


def solution(mesh):
    return jax.shard_map(
        shards,
        mesh=mesh,
        in_specs=(P("kloop", None, None), P(), P(None, None, "pair"), P(), P()),
        out_specs=P("kloop", None, "pair", None),
        check_vma=False,
    )
```

```python
import jax
import jax.numpy as jnp
from jax import lax
from jax.sharding import PartitionSpec as P
from jax.experimental import pallas as pl
from jax.experimental.pallas import tpu as pltpu

NV = 16
NC = 16
S = 2


def from_behind(value, axis, steps):
    count = lax.axis_size(axis)
    pairs = [(source, (source + steps) % count) for source in range(count)]
    return lax.ppermute(value, axis, pairs)


def products(left_bands, right_bands):
    prod = left_bands.astype(jnp.float32)[..., :, None, :] * right_bands.astype(jnp.float32)[..., None, :, :]
    lead = prod.shape[:-3]
    return prod.astype(jnp.bfloat16).reshape(*lead, prod.shape[-3] * prod.shape[-2], prod.shape[-1])


def products_t(left_bands, right_bands):
    left_t = jnp.swapaxes(left_bands, -1, -2).astype(jnp.float32)
    right_t = jnp.swapaxes(right_bands, -1, -2).astype(jnp.float32)
    prod = (left_t[..., :, None] * right_t[..., None, :]).astype(jnp.bfloat16)
    return prod.reshape(*prod.shape[:-2], prod.shape[-2] * prod.shape[-1])


def fields(left_bands, right_bands, fit):
    prod = products(left_bands, right_bands)
    return jnp.einsum("...pm,mg->...pg", prod, fit, preferred_element_type=jnp.float32).astype(jnp.bfloat16)


def nt(left, right):
    return lax.dot_general(left, right, (((1,), (1,)), ((), ())), preferred_element_type=jnp.float32)


def direct_kernel(q_ref, cond_pairs_ref, vale_pairs_ref, fit_ref, fit_part_ref, screen_ref, out_ref):
    q = q_ref[pl.program_id(0)]
    cond_t = jnp.dot(fit_ref[...], cond_pairs_ref[0], preferred_element_type=jnp.float32).astype(jnp.bfloat16)
    s_all = screen_ref[...].reshape(screen_ref.shape[0] * screen_ref.shape[1], screen_ref.shape[2])
    every = jnp.dot(s_all, cond_t, preferred_element_type=jnp.float32).astype(jnp.bfloat16)
    width = fit_part_ref.shape[0]
    rows_all = screen_ref.shape[0] * screen_ref.shape[1]
    row = lax.broadcasted_iota(jnp.int32, (width, rows_all), 0)
    col = lax.broadcasted_iota(jnp.int32, (width, rows_all), 1)
    pick = jnp.where(col == row * screen_ref.shape[1] + q, 1.0, 0.0).astype(jnp.bfloat16)
    screened_t = jnp.dot(pick, every, preferred_element_type=jnp.float32).astype(jnp.bfloat16)
    vale_t = jnp.dot(fit_part_ref[...], vale_pairs_ref[0], preferred_element_type=jnp.float32).astype(jnp.bfloat16)
    terms = lax.dot_general(vale_t, screened_t, (((0,), (0,)), ((), ())), preferred_element_type=jnp.float32)
    out_ref[0] = terms.astype(jnp.bfloat16)


def direct_terms(q, cond_pairs, vale_pairs, fit_t, fit_part_t, screen_t):
    blocks, mu, rows = cond_pairs.shape
    vrows = vale_pairs.shape[2]
    full = lambda shape: pl.BlockSpec(shape, lambda b, q: (0,) * len(shape))
    return pl.pallas_call(
        direct_kernel,
        out_shape=jax.ShapeDtypeStruct((blocks, vrows, rows), jnp.bfloat16),
        grid_spec=pltpu.PrefetchScalarGridSpec(
            num_scalar_prefetch=1,
            grid=(blocks,),
            in_specs=[
                pl.BlockSpec((1, mu, rows), lambda b, q: (b, 0, 0)),
                pl.BlockSpec((1, mu, vrows), lambda b, q: (b, 0, 0)),
                full(fit_t.shape),
                full(fit_part_t.shape),
                full(screen_t.shape),
            ],
            out_specs=pl.BlockSpec((1, vrows, rows), lambda b, q: (b, 0, 0)),
        ),
    )(q, cond_pairs, vale_pairs, fit_t, fit_part_t, screen_t)


def shards(orbitals, fitting, screen, coulomb, qindex):
    per_dev = orbitals.shape[0]
    npair = lax.axis_size("pair")
    pair_index = lax.axis_index("pair")
    loop_index = lax.axis_index("kloop")
    width = screen.shape[2]
    ng = screen.shape[1]
    vr = NV // npair

    rows = jnp.stack([from_behind(orbitals, "kloop", -s) for s in range(1, S + 1)], 0)
    cols = jnp.broadcast_to(orbitals[None], rows.shape)

    own = fields(orbitals[:, :NV], orbitals[:, NV:], fitting)

    blocks = S * per_dev
    cond_pairs = products_t(rows[:, :, NV:], cols[:, :, NV:]).reshape(blocks, -1, NC * NC)
    vale_pairs = products_t(rows[:, :, :NV], cols[:, :, :NV]).reshape(blocks, -1, NV * NV)
    fit_t = fitting.T
    fit_part_t = lax.dynamic_slice_in_dim(fit_t, pair_index * width, width, 0)

    nq = screen.shape[0]
    qs = jnp.stack([qindex[loop_index * per_dev + lk, s] for s in range(S) for lk in range(per_dev)])
    qs = jnp.clip(qs, 0, nq - 1)
    terms = direct_terms(qs, cond_pairs, vale_pairs, fit_t, fit_part_t, jnp.transpose(screen, (2, 0, 1)))
    terms = terms.reshape(S, per_dev, npair, vr * NV, NC * NC)
    terms = jnp.moveaxis(terms, 2, 0)
    got = lax.all_to_all(terms, "pair", 0, 0, tiled=True)
    dsum = jnp.sum(got.astype(jnp.float32), axis=0)
    direct = dsum.reshape(S, per_dev, vr, NV, NC, NC).transpose(0, 1, 2, 4, 3, 5).reshape(S, per_dev, vr * NC, NV * NC)

    row_chosen = lax.dynamic_slice_in_dim(rows, pair_index * vr, vr, 2)
    rowf = fields(row_chosen, rows[:, :, NV:], fitting)
    weighted = (rowf.astype(jnp.float32) * coulomb).astype(jnp.bfloat16)
    exchange = jnp.einsum("abpg,bqg->abpq", weighted, own, preferred_element_type=jnp.float32)
    out = (2.0 * exchange - direct).astype(jnp.bfloat16)
    return jnp.swapaxes(out, 0, 1)


def solution(mesh):
    return jax.shard_map(
        shards,
        mesh=mesh,
        in_specs=(P("kloop", None, None), P(), P(None, None, "pair"), P(), P()),
        out_specs=P("kloop", None, "pair", None),
        check_vma=False,
    )
```

```python
import jax
import jax.numpy as jnp
from jax import lax
from jax.sharding import PartitionSpec as P

NV = 16
NC = 16
S = 2


def from_behind(value, axis, steps):
    count = lax.axis_size(axis)
    pairs = [(source, (source + steps) % count) for source in range(count)]
    return lax.ppermute(value, axis, pairs)


def products(left_bands, right_bands):
    prod = left_bands.astype(jnp.float32)[..., :, None, :] * right_bands.astype(jnp.float32)[..., None, :, :]
    lead = prod.shape[:-3]
    return prod.astype(jnp.bfloat16).reshape(*lead, prod.shape[-3] * prod.shape[-2], prod.shape[-1])


def fields(left_bands, right_bands, fit):
    prod = products(left_bands, right_bands)
    return jnp.einsum("...pm,mg->...pg", prod, fit, preferred_element_type=jnp.float32).astype(jnp.bfloat16)


def shards(orbitals, fitting, screen, coulomb, qindex):
    per_dev = orbitals.shape[0]
    npair = lax.axis_size("pair")
    pair_index = lax.axis_index("pair")
    loop_index = lax.axis_index("kloop")
    width = screen.shape[2]
    ng = screen.shape[1]
    vr = NV // npair
    fitting_part = lax.dynamic_slice_in_dim(fitting, pair_index * width, width, 1)

    rows = jnp.stack([from_behind(orbitals, "kloop", -s) for s in range(1, S + 1)], 0)
    cols = jnp.broadcast_to(orbitals[None], rows.shape)

    own = fields(orbitals[:, :NV], orbitals[:, NV:], fitting)

    cond = fields(rows[:, :, NV:], cols[:, :, NV:], fitting)
    vale = fields(rows[:, :, :NV], cols[:, :, :NV], fitting_part)

    screen2d = screen.reshape(screen.shape[0] * ng, width)
    qs = lax.dynamic_slice_in_dim(qindex, loop_index * per_dev, per_dev, 0)
    screened = []
    for s in range(S):
        row_s = []
        for lk in range(per_dev):
            q = qs[lk, s]
            inter = lax.dynamic_slice_in_dim(screen2d, q * ng, ng, 0)
            row_s.append(jnp.dot(cond[s, lk], inter, preferred_element_type=jnp.float32).astype(jnp.bfloat16))
        screened.append(jnp.stack(row_s, 0))
    screened = jnp.stack(screened, 0)

    terms = jnp.einsum("abpg,abqg->abpq", vale, screened, preferred_element_type=jnp.float32).astype(jnp.bfloat16)
    terms = terms.reshape(S, per_dev, npair, vr * NV, NC * NC)
    terms = jnp.moveaxis(terms, 2, 0)
    got = lax.all_to_all(terms, "pair", 0, 0, tiled=True)
    dsum = jnp.sum(got.astype(jnp.float32), axis=0)
    direct = dsum.reshape(S, per_dev, vr, NV, NC, NC).transpose(0, 1, 2, 4, 3, 5).reshape(S, per_dev, vr * NC, NV * NC)

    row_chosen = lax.dynamic_slice_in_dim(rows, pair_index * vr, vr, 2)
    rowf = fields(row_chosen, rows[:, :, NV:], fitting)
    weighted = (rowf.astype(jnp.float32) * coulomb).astype(jnp.bfloat16)
    exchange = jnp.einsum("abpg,bqg->abpq", weighted, own, preferred_element_type=jnp.float32)
    out = (2.0 * exchange - direct).astype(jnp.bfloat16)
    return jnp.swapaxes(out, 0, 1)


def solution(mesh):
    return jax.shard_map(
        shards,
        mesh=mesh,
        in_specs=(P("kloop", None, None), P(), P(None, None, "pair"), P(), P()),
        out_specs=P("kloop", None, "pair", None),
        check_vma=False,
    )
```

```python
import jax
import jax.numpy as jnp
from jax import lax
from jax.sharding import PartitionSpec as P

NV = 16
NC = 16
S = 2


def from_behind(value, axis, steps):
    count = lax.axis_size(axis)
    pairs = [(source, (source + steps) % count) for source in range(count)]
    return lax.ppermute(value, axis, pairs)


def products(left_bands, right_bands):
    prod = left_bands.astype(jnp.float32)[..., :, None, :] * right_bands.astype(jnp.float32)[..., None, :, :]
    lead = prod.shape[:-3]
    return prod.astype(jnp.bfloat16).reshape(*lead, prod.shape[-3] * prod.shape[-2], prod.shape[-1])


def fields(left_bands, right_bands, fit):
    prod = products(left_bands, right_bands)
    return jnp.einsum("...pm,mg->...pg", prod, fit, preferred_element_type=jnp.float32).astype(jnp.bfloat16)


def shards(orbitals, fitting, screen, coulomb, qindex):
    per_dev = orbitals.shape[0]
    npair = lax.axis_size("pair")
    pair_index = lax.axis_index("pair")
    loop_index = lax.axis_index("kloop")
    width = screen.shape[2]
    ng = screen.shape[1]
    vr = NV // npair
    fitting_part = lax.dynamic_slice_in_dim(fitting, pair_index * width, width, 1)

    rows = jnp.stack([from_behind(orbitals, "kloop", -s) for s in range(1, S + 1)], 0)
    cols = jnp.broadcast_to(orbitals[None], rows.shape)

    own = fields(orbitals[:, :NV], orbitals[:, NV:], fitting)

    cond = fields(rows[:, :, NV:], cols[:, :, NV:], fitting)
    vale = fields(rows[:, :, :NV], cols[:, :, :NV], fitting_part)

    screen2d = screen.reshape(screen.shape[0] * ng, width)
    qs = lax.dynamic_slice_in_dim(qindex, loop_index * per_dev, per_dev, 0)
    screened = []
    for s in range(S):
        row_s = []
        for lk in range(per_dev):
            q = qs[lk, s]
            inter = lax.dynamic_slice_in_dim(screen2d, q * ng, ng, 0)
            row_s.append(jnp.dot(cond[s, lk], inter, preferred_element_type=jnp.float32).astype(jnp.bfloat16))
        screened.append(jnp.stack(row_s, 0))
    screened = jnp.stack(screened, 0)

    terms = jnp.einsum("abpg,abqg->abpq", vale, screened, preferred_element_type=jnp.float32).astype(jnp.bfloat16)
    terms = terms.reshape(S, per_dev, npair, vr * NV, NC * NC)
    terms = jnp.moveaxis(terms, 2, 0)
    got = lax.all_to_all(terms, "pair", 0, 0, tiled=True)
    dsum = jnp.sum(got.astype(jnp.float32), axis=0)
    direct = dsum.reshape(S, per_dev, vr, NV, NC, NC).transpose(0, 1, 2, 4, 3, 5).reshape(S, per_dev, vr * NC, NV * NC)

    row_chosen = lax.dynamic_slice_in_dim(rows, pair_index * vr, vr, 2)
    rowf = fields(row_chosen, rows[:, :, NV:], fitting)
    weighted = (rowf.astype(jnp.float32) * coulomb).astype(jnp.bfloat16)
    exchange = jnp.einsum("abpg,bqg->abpq", weighted, own, preferred_element_type=jnp.float32)
    exchange = lax.optimization_barrier(exchange)
    out = (2.0 * exchange - direct).astype(jnp.bfloat16)
    return jnp.swapaxes(out, 0, 1)


def solution(mesh):
    return jax.shard_map(
        shards,
        mesh=mesh,
        in_specs=(P("kloop", None, None), P(), P(None, None, "pair"), P(), P()),
        out_specs=P("kloop", None, "pair", None),
        check_vma=False,
    )
```

```python
import jax
import jax.numpy as jnp
from jax import lax
from jax.sharding import PartitionSpec as P

NV = 16
NC = 16
S = 2


def from_behind(value, axis, steps):
    count = lax.axis_size(axis)
    pairs = [(source, (source + steps) % count) for source in range(count)]
    return lax.ppermute(value, axis, pairs)


def products(left_bands, right_bands):
    prod = left_bands.astype(jnp.float32)[..., :, None, :] * right_bands.astype(jnp.float32)[..., None, :, :]
    lead = prod.shape[:-3]
    return prod.astype(jnp.bfloat16).reshape(*lead, prod.shape[-3] * prod.shape[-2], prod.shape[-1])


def fields(left_bands, right_bands, fit):
    prod = products(left_bands, right_bands)
    return jnp.einsum("...pm,mg->...pg", prod, fit, preferred_element_type=jnp.float32).astype(jnp.bfloat16)


def shards(orbitals, fitting, screen, coulomb, qindex):
    per_dev = orbitals.shape[0]
    npair = lax.axis_size("pair")
    pair_index = lax.axis_index("pair")
    loop_index = lax.axis_index("kloop")
    width = screen.shape[2]
    ng = screen.shape[1]
    vr = NV // npair
    fitting_part = lax.dynamic_slice_in_dim(fitting, pair_index * width, width, 1)

    rows = jnp.stack([from_behind(orbitals, "kloop", -s) for s in range(1, S + 1)], 0)
    cols = jnp.broadcast_to(orbitals[None], rows.shape)

    own = fields(orbitals[:, :NV], orbitals[:, NV:], fitting)

    cond = fields(rows[:, :, NV:], cols[:, :, NV:], fitting)
    vale = fields(rows[:, :, :NV], cols[:, :, :NV], fitting_part)

    screen2d = screen.reshape(screen.shape[0] * ng, width)
    screened = []
    for s in range(S):
        row_s = []
        for lk in range(per_dev):
            q = qindex[loop_index * per_dev + lk, s]
            inter = lax.dynamic_slice_in_dim(screen2d, q * ng, ng, 0)
            row_s.append(jnp.dot(cond[s, lk], inter, preferred_element_type=jnp.float32).astype(jnp.bfloat16))
        screened.append(jnp.stack(row_s, 0))
    screened = jnp.stack(screened, 0)

    terms = jnp.einsum("abpg,abqg->abpq", vale, screened, preferred_element_type=jnp.float32).astype(jnp.bfloat16)
    terms = terms.reshape(S, per_dev, npair, vr * NV, NC * NC)
    terms = jnp.moveaxis(terms, 2, 0)
    got = lax.all_to_all(terms, "pair", 0, 0, tiled=True)
    dsum = jnp.sum(got.astype(jnp.float32), axis=0)

    row_chosen = lax.dynamic_slice_in_dim(rows, pair_index * vr, vr, 2)
    rowf = fields(row_chosen, rows[:, :, NV:], fitting)
    weighted = (rowf.astype(jnp.float32) * coulomb).astype(jnp.bfloat16)
    exchange = jnp.einsum("abpg,bqg->abpq", weighted, own, preferred_element_type=jnp.float32)
    exchange = exchange.reshape(S, per_dev, vr, NC, NV, NC).transpose(0, 1, 2, 4, 3, 5).reshape(dsum.shape)
    out = (2.0 * exchange - dsum).astype(jnp.bfloat16)
    out = out.reshape(S, per_dev, vr, NV, NC, NC).transpose(0, 1, 2, 4, 3, 5).reshape(S, per_dev, vr * NC, NV * NC)
    return jnp.swapaxes(out, 0, 1)


def solution(mesh):
    return jax.shard_map(
        shards,
        mesh=mesh,
        in_specs=(P("kloop", None, None), P(), P(None, None, "pair"), P(), P()),
        out_specs=P("kloop", None, "pair", None),
        check_vma=False,
    )
```

```python
import jax
import jax.numpy as jnp
from jax import lax
from jax.sharding import PartitionSpec as P

NV = 16
NC = 16
S = 2


def from_behind(value, axis, steps):
    count = lax.axis_size(axis)
    pairs = [(source, (source + steps) % count) for source in range(count)]
    return lax.ppermute(value, axis, pairs)


def products(left_bands, right_bands):
    prod = left_bands.astype(jnp.float32)[..., :, None, :] * right_bands.astype(jnp.float32)[..., None, :, :]
    lead = prod.shape[:-3]
    return prod.astype(jnp.bfloat16).reshape(*lead, prod.shape[-3] * prod.shape[-2], prod.shape[-1])


def fields(left_bands, right_bands, fit):
    prod = products(left_bands, right_bands)
    return jnp.einsum("...pm,mg->...pg", prod, fit, preferred_element_type=jnp.float32).astype(jnp.bfloat16)


def shards(orbitals, fitting, screen, coulomb, qindex):
    per_dev = orbitals.shape[0]
    npair = lax.axis_size("pair")
    pair_index = lax.axis_index("pair")
    loop_index = lax.axis_index("kloop")
    width = screen.shape[2]
    ng = screen.shape[1]
    vr = NV // npair
    fitting_part = lax.dynamic_slice_in_dim(fitting, pair_index * width, width, 1)

    rows = jnp.stack([from_behind(orbitals, "kloop", -s) for s in range(1, S + 1)], 0)
    cols = jnp.broadcast_to(orbitals[None], rows.shape)

    own = fields(orbitals[:, :NV], orbitals[:, NV:], fitting)

    cond = fields(rows[:, :, NV:], cols[:, :, NV:], fitting)
    vale = fields(rows[:, :, :NV], cols[:, :, :NV], fitting_part)

    screen2d = screen.reshape(screen.shape[0] * ng, width)
    screened = []
    for s in range(S):
        row_s = []
        for lk in range(per_dev):
            q = qindex[loop_index * per_dev + lk, s]
            inter = lax.dynamic_slice_in_dim(screen2d, q * ng, ng, 0)
            row_s.append(jnp.dot(cond[s, lk], inter, preferred_element_type=jnp.float32).astype(jnp.bfloat16))
        screened.append(jnp.stack(row_s, 0))
    screened = jnp.stack(screened, 0)

    terms = jnp.einsum("abpg,abqg->abpq", vale, screened, preferred_element_type=jnp.float32).astype(jnp.bfloat16)
    terms = terms.reshape(S, per_dev, npair, vr * NV, NC * NC)
    terms = jnp.moveaxis(terms, 2, 0)
    got = lax.all_to_all(terms, "pair", 0, 0, tiled=True)
    dsum = jnp.sum(got.astype(jnp.float32), axis=0)
    direct = jnp.swapaxes(dsum.reshape(S * per_dev * vr, NV, NC, NC), 1, 2).reshape(S, per_dev, vr * NC, NV * NC)

    row_chosen = lax.dynamic_slice_in_dim(rows, pair_index * vr, vr, 2)
    rowf = fields(row_chosen, rows[:, :, NV:], fitting)
    weighted = (rowf.astype(jnp.float32) * coulomb).astype(jnp.bfloat16)
    exchange = jnp.einsum("abpg,bqg->abpq", weighted, own, preferred_element_type=jnp.float32)
    out = (2.0 * exchange - direct).astype(jnp.bfloat16)
    return jnp.swapaxes(out, 0, 1)


def solution(mesh):
    return jax.shard_map(
        shards,
        mesh=mesh,
        in_specs=(P("kloop", None, None), P(), P(None, None, "pair"), P(), P()),
        out_specs=P("kloop", None, "pair", None),
        check_vma=False,
    )
```
